256 devices in a mesh: dp: 16 (over y_hi, z), seq: 16 (over x, y_lo, core).
Axes of the slice: x: 4, y: 4 (y_hi: 2, y_lo: 2; y = y_hi * 2 + y_lo), z: 8, core: 2. Of those that a mesh axis runs over, the one named last changes fastest.
Arguments:
- queries: bfloat16 [16, 2048, 2048], P('dp', 'seq'), may hold values from -6 to 6
- key_states: bfloat16 [16, 2048, 2048], P('dp', 'seq'), may hold values from -6 to 6
- value_states: bfloat16 [16, 2048, 2048], P('dp', 'seq'), may hold values from -6 to 6
- cotangent: bfloat16 [16, 2048, 2048], P('dp', 'seq'), may hold values from -6 to 6
- filter_taps: float32 [7, 2048], replicated, may hold values from -3 to 3
Outputs:
- conv_output: bfloat16 [16, 2048, 2048], P('dp', 'seq')
- grad_queries: bfloat16 [16, 2048, 2048], P('dp', 'seq')
- grad_keys: bfloat16 [16, 2048, 2048], P('dp', 'seq')
- grad_values: bfloat16 [16, 2048, 2048], P('dp', 'seq')
- filter_gradient: float32 [7, 2048], replicated
The draws below stay inside these ranges and needn't reach their ends.
All inputs are finite; a program needn't handle non-finite values.
Results may differ from the reference program's by a relative error of at most 0.015.
Values may be sent and summed in bfloat16 or wider, within the bound.
No kernel may reach another device: no remote copies, remote signals or barrier semaphores. Data moves between devices by JAX's collectives and lax.ppermute only.
A program may use at most 128 MiB of HBM per device.

```python
import jax
import jax.numpy as jnp
from jax import lax

HEADS = 16
HD = 128
TAPS = 7
TOK_DEV = 128
LEN = 2048
WINDOWS = 16
N_SEQ = 16


def draw_queries(key, part):
    values = 1.5 * jax.random.normal(jax.random.fold_in(key, 11), (WINDOWS, LEN, HEADS * HD), jnp.float32)
    values = jnp.clip(values, -6.0, 6.0)
    return values.astype(jnp.bfloat16)


def draw_key_states(key, part):
    values = 1.5 * jax.random.normal(jax.random.fold_in(key, 13), (WINDOWS, LEN, HEADS * HD), jnp.float32)
    values = jnp.clip(values, -6.0, 6.0)
    return values.astype(jnp.bfloat16)


def steps_of(stream_key, dims, split, low, largest):
    def one(axis_at, parts):
        steps = jax.random.uniform(jax.random.fold_in(jax.random.fold_in(stream_key, 6), axis_at), (parts,), jnp.float32, low / len(split), largest / len(split))
        return jnp.repeat(jnp.exp(steps), dims[axis_at] // parts).reshape((-1,) + (1,) * (len(dims) - axis_at - 1))

    gain = one(*split[0])
    for cut in split[1:]:
        gain = gain * one(*cut)
    return gain


def bell_draw(rng, shape, scale, limit, cuts=(), held_as=jnp.bfloat16):
    values = scale * jax.random.normal(rng, shape, jnp.float32)
    if cuts:
        values = values * steps_of(rng, shape, cuts, -0.22, 0.18)
    return jnp.clip(values, -limit, limit).astype(held_as)


def setup_inputs(seed: int = 0) -> dict:
    keys = jax.random.split(jax.random.key(seed), 6)
    queries = draw_queries(jax.random.fold_in(keys[5], 71), 0)
    key_states = draw_key_states(jax.random.fold_in(keys[5], 71), 0)
    value_states = bell_draw(keys[2], (WINDOWS, LEN, HEADS * HD), 1.0, 6.0, ((0, 16), (1, 16)))
    cotangent = bell_draw(keys[3], (WINDOWS, LEN, HEADS * HD), 1.0, 6.0, ((0, 16), (1, 16)))
    filter_taps = bell_draw(keys[4], (TAPS, HEADS * HD), 0.5, 3.0, (), jnp.float32)
    return dict(queries=queries, key_states=key_states, value_states=value_states, cotangent=cotangent, filter_taps=filter_taps)


def block_sum(weights, rows_in):
    length = weights.shape[1]
    block_grouped = weights.astype(jnp.float32).reshape(N_SEQ, TOK_DEV, length)
    row_tiles_list = rows_in.astype(jnp.float32).reshape(N_SEQ, TOK_DEV, rows_in.shape[1])
    running_sums = jnp.einsum("kzt,kzc->ktc", block_grouped, row_tiles_list).astype(jnp.bfloat16)
    running_sums = lax.optimization_barrier(running_sums)
    return jnp.sum(running_sums.astype(jnp.float32), 0).astype(jnp.bfloat16)


def head_pass(items):
    q_head, k_head, v_head, d_head = items
    length = q_head.shape[0]
    score_scale = HD ** -0.5
    positions = jnp.arange(length, dtype=jnp.int32)
    visible = positions[:, None] >= positions[None, :]
    scores = jnp.dot(q_head, k_head.T, preferred_element_type=jnp.float32) * score_scale
    row_top = jnp.max(jnp.where(visible, scores, -jnp.inf), -1, keepdims=True)
    raw = jnp.where(visible, jnp.exp(scores - row_top), 0.0)
    probs = raw / jnp.sum(raw, -1, keepdims=True)
    probs_low = probs.astype(jnp.bfloat16)
    attended = jnp.dot(probs_low, v_head, preferred_element_type=jnp.float32).astype(jnp.bfloat16)
    dprob = jnp.dot(d_head, v_head.T, preferred_element_type=jnp.float32)
    row_delta = jnp.sum(probs * dprob, -1, keepdims=True)
    dscore = (probs * (dprob - row_delta) * score_scale).astype(jnp.bfloat16)
    grad_q = jnp.dot(dscore, k_head, preferred_element_type=jnp.float32).astype(jnp.bfloat16)
    grad_k = block_sum(dscore, q_head)
    grad_v = block_sum(probs_low, d_head)
    return attended, grad_q, grad_k, grad_v


def split_heads(matrix):
    return matrix.reshape(LEN, HEADS, HD).transpose(1, 0, 2)


def merge_heads(stacked):
    return stacked.transpose(1, 0, 2).reshape(LEN, HEADS * HD)


def window_pass(items, filter_taps):
    q_win, k_win, v_win, g_win = items
    half_width = (TAPS - 1) // 2
    grad_sum = jnp.zeros((LEN, HEADS * HD), jnp.float32)
    for tap_index in range(TAPS):
        grad_sum = grad_sum + filter_taps[tap_index] * jnp.roll(g_win, tap_index - half_width, axis=0).astype(jnp.float32)
    grad_attn = grad_sum.astype(jnp.bfloat16)
    results = lax.map(head_pass, (split_heads(q_win), split_heads(k_win), split_heads(v_win), split_heads(grad_attn)))
    attended = merge_heads(results[0])
    conv_sum = jnp.zeros((LEN, HEADS * HD), jnp.float32)
    filter_rows = []
    for tap_index in range(TAPS):
        moved = jnp.roll(attended, half_width - tap_index, axis=0).astype(jnp.float32)
        conv_sum = conv_sum + filter_taps[tap_index] * moved
        filter_rows.append(jnp.sum(moved * g_win.astype(jnp.float32), 0))
    return (conv_sum.astype(jnp.bfloat16), merge_heads(results[1]), merge_heads(results[2]),
            merge_heads(results[3]), jnp.stack(filter_rows, 0))


def reference(queries, key_states, value_states, cotangent, filter_taps):
    results = lax.map(lambda items: window_pass(items, filter_taps), (queries, key_states, value_states, cotangent))
    return results[0], results[1], results[2], results[3], jnp.sum(results[4], 0)
```

```python
import math

import jax
import jax.numpy as jnp
import numpy as np
from jax import lax
from jax.sharding import Mesh
from jax.sharding import PartitionSpec as P

HD = 128
TAPS = 7
GROUP_HEADS = 2

SEQ = ("sc", "core")


def padded(value, width):
    peers = lax.axis_size("sc") * lax.axis_size("core")
    length = value.shape[0]
    up = [(i, (i + 1) % peers) for i in range(peers)]
    down = [(j, i) for i, j in up]
    before = lax.ppermute(value[length - width :], SEQ, up)
    after = lax.ppermute(value[:width], SEQ, down)
    return jnp.concatenate([before, value, after], axis=0)


def to_chip_rows(value):
    rows, channels = value.shape
    split = value.reshape(rows, 2, channels // 2)
    return lax.all_to_all(split, "core", 1, 0, tiled=True).reshape(2 * rows, channels // 2)


def from_chip_rows(value):
    rows2, half = value.shape
    split = value.reshape(2, rows2 // 2, 1, half)
    out = lax.all_to_all(split, "core", 0, 2, tiled=True)
    return out.reshape(rows2 // 2, 2 * half)


def on_device(queries, key_states, value_states, cotangent, filter_taps):
    tok_rows = queries.shape[1]
    channels = queries.shape[2]
    chips = lax.axis_size("sc")
    seq_total = tok_rows * chips * 2
    chip_rows = 2 * tok_rows
    half_channels = channels // 2
    head_count = half_channels // HD
    group_width = GROUP_HEADS * HD
    group_count = head_count // GROUP_HEADS
    score_scale = HD ** (-0.5)
    half_width = (TAPS - 1) // 2
    local_q = queries[0]
    local_k = key_states[0]
    local_v = value_states[0]
    local_g = cotangent[0]
    grad_pad = padded(local_g, half_width)
    grad_sum = jnp.zeros((tok_rows, channels), jnp.float32)
    for tap_index in range(TAPS):
        start_row = 2 * half_width - tap_index
        grad_sum = grad_sum + filter_taps[tap_index] * grad_pad[
            start_row : start_row + tok_rows
        ].astype(jnp.float32)
    grad_attn = grad_sum.astype(jnp.bfloat16)

    chip_q = to_chip_rows(local_q)
    chip_k = to_chip_rows(local_k)
    chip_v = to_chip_rows(local_v)
    chip_d = to_chip_rows(grad_attn)

    chip_index = lax.axis_index("sc")
    query_pos = chip_index * chip_rows + jnp.arange(chip_rows, dtype=jnp.int32)
    key_pos = jnp.arange(seq_total, dtype=jnp.int32)
    visible = query_pos[:, None] >= key_pos[None, :]

    attended_parts, grad_q_parts, key_parts, value_parts = [], [], [], []
    for group_index in range(group_count):
        cols = slice(group_index * group_width, (group_index + 1) * group_width)
        k_all = lax.all_gather(chip_k[:, cols], "sc", axis=0, tiled=True)
        v_all = lax.all_gather(chip_v[:, cols], "sc", axis=0, tiled=True)
        q_part = chip_q[:, cols].reshape(chip_rows, GROUP_HEADS, HD)
        d_part = chip_d[:, cols].reshape(chip_rows, GROUP_HEADS, HD)
        k_part = k_all.reshape(seq_total, GROUP_HEADS, HD)
        v_part = v_all.reshape(seq_total, GROUP_HEADS, HD)
        scores = (
            jnp.einsum("thd,uhd->htu", q_part, k_part, preferred_element_type=jnp.float32)
            * score_scale
        )
        row_top = jnp.max(jnp.where(visible, scores, -jnp.inf), -1, keepdims=True)
        raw = jnp.where(visible, jnp.exp(scores - row_top), 0.0)
        row_total = jnp.sum(raw, -1, keepdims=True)
        probs = raw / row_total
        probs_low = probs.astype(jnp.bfloat16)
        attended = jnp.einsum("htu,uhd->thd", probs_low, v_part, preferred_element_type=jnp.float32)
        attended_parts.append(attended.astype(jnp.bfloat16).reshape(chip_rows, group_width))
        dprob = jnp.einsum("thd,uhd->htu", d_part, v_part, preferred_element_type=jnp.float32)
        row_delta = jnp.sum(probs * dprob, -1, keepdims=True)
        dscore = (probs * (dprob - row_delta) * score_scale).astype(jnp.bfloat16)
        grad_q = jnp.einsum("htu,uhd->thd", dscore, k_part, preferred_element_type=jnp.float32)
        grad_q_parts.append(grad_q.astype(jnp.bfloat16).reshape(chip_rows, group_width))
        key_term = jnp.einsum("htu,thd->uhd", dscore, q_part, preferred_element_type=jnp.float32)
        value_term = jnp.einsum("htu,thd->uhd", probs_low, d_part, preferred_element_type=jnp.float32)
        key_parts.append(
            lax.psum_scatter(
                key_term.astype(jnp.bfloat16).reshape(seq_total, group_width),
                "sc", scatter_dimension=0, tiled=True,
            )
        )
        value_parts.append(
            lax.psum_scatter(
                value_term.astype(jnp.bfloat16).reshape(seq_total, group_width),
                "sc", scatter_dimension=0, tiled=True,
            )
        )

    attn_out = from_chip_rows(jnp.concatenate(attended_parts, axis=1))
    grad_queries = from_chip_rows(jnp.concatenate(grad_q_parts, axis=1))
    grad_keys = from_chip_rows(jnp.concatenate(key_parts, axis=1))
    grad_values = from_chip_rows(jnp.concatenate(value_parts, axis=1))

    out_pad = padded(attn_out, half_width)
    conv_sum = jnp.zeros((tok_rows, channels), jnp.float32)
    filter_rows = []
    local_gf = local_g.astype(jnp.float32)
    for tap_index in range(TAPS):
        moved = out_pad[tap_index : tap_index + tok_rows].astype(jnp.float32)
        conv_sum = conv_sum + filter_taps[tap_index] * moved
        filter_rows.append(jnp.sum(moved * local_gf, 0))
    filter_gradient = lax.psum(jnp.stack(filter_rows, 0), ("dp", "sc", "core"))
    conv_output = conv_sum.astype(jnp.bfloat16)
    return (
        conv_output[None],
        grad_queries[None],
        grad_keys[None],
        grad_values[None],
        filter_gradient,
    )


def solution(mesh):
    devices = np.asarray(mesh.devices)
    dp_size, seq_size = devices.shape
    split_mesh = Mesh(devices.reshape(dp_size, seq_size // 2, 2), ("dp", "sc", "core"))
    block = P("dp", SEQ, None)
    in_specs = (block, block, block, block, P())
    out_specs = (block, block, block, block, P())
    return jax.shard_map(
        on_device, mesh=split_mesh, in_specs=in_specs, out_specs=out_specs, check_vma=False
    )
```

```python
import math

import jax
import jax.numpy as jnp
import numpy as np
from jax import lax
from jax.sharding import Mesh
from jax.sharding import PartitionSpec as P

HD = 128
TAPS = 7
GROUP_HEADS = 2

SEQ = ("sc", "core")


def padded(value, width):
    peers = lax.axis_size("sc") * lax.axis_size("core")
    length = value.shape[0]
    up = [(i, (i + 1) % peers) for i in range(peers)]
    down = [(j, i) for i, j in up]
    before = lax.ppermute(value[length - width :], SEQ, up)
    after = lax.ppermute(value[:width], SEQ, down)
    return jnp.concatenate([before, value, after], axis=0)


def to_chip_rows(value):
    rows, channels = value.shape
    split = value.reshape(rows, 2, channels // 2)
    return lax.all_to_all(split, "core", 1, 0, tiled=True).reshape(2 * rows, channels // 2)


def from_chip_rows(value):
    rows2, half = value.shape
    split = value.reshape(2, rows2 // 2, 1, half)
    out = lax.all_to_all(split, "core", 0, 2, tiled=True)
    return out.reshape(rows2 // 2, 2 * half)


def butterfly_sum(value):
    axes = ("dp", "sc", "core")
    peers = 1
    for axis in axes:
        peers *= lax.axis_size(axis)
    bit = 1
    while bit < peers:
        pairs = [(i, i ^ bit) for i in range(peers)]
        value = value + lax.ppermute(value, axes, pairs)
        bit *= 2
    return value


def on_device(queries, key_states, value_states, cotangent, filter_taps):
    tok_rows = queries.shape[1]
    channels = queries.shape[2]
    chips = lax.axis_size("sc")
    seq_total = tok_rows * chips * 2
    chip_rows = 2 * tok_rows
    half_channels = channels // 2
    head_count = half_channels // HD
    group_width = GROUP_HEADS * HD
    group_count = head_count // GROUP_HEADS
    score_scale = HD ** (-0.5)
    half_width = (TAPS - 1) // 2
    local_q = queries[0]
    local_k = key_states[0]
    local_v = value_states[0]
    local_g = cotangent[0]
    grad_pad = padded(local_g, half_width)
    grad_sum = jnp.zeros((tok_rows, channels), jnp.float32)
    for tap_index in range(TAPS):
        start_row = 2 * half_width - tap_index
        grad_sum = grad_sum + filter_taps[tap_index] * grad_pad[
            start_row : start_row + tok_rows
        ].astype(jnp.float32)
    grad_attn = grad_sum.astype(jnp.bfloat16)

    stacked = jnp.stack([local_q, local_k, local_v, grad_attn], 0)
    stacked = stacked.reshape(4, tok_rows, 2, half_channels)
    stacked = lax.all_to_all(stacked, "core", 2, 1, tiled=True)
    stacked = stacked.reshape(4, chip_rows, half_channels)
    chip_q, chip_k, chip_v, chip_d = stacked[0], stacked[1], stacked[2], stacked[3]

    kv_all = lax.all_gather(
        jnp.concatenate([chip_k, chip_v], axis=1), "sc", axis=0, tiled=True
    )
    k_heads = kv_all[:, :half_channels].reshape(seq_total, head_count, HD)
    v_heads = kv_all[:, half_channels:].reshape(seq_total, head_count, HD)
    q_heads = chip_q.reshape(chip_rows, head_count, HD)
    d_heads = chip_d.reshape(chip_rows, head_count, HD)

    chip_index = lax.axis_index("sc")
    query_pos = chip_index * chip_rows + jnp.arange(chip_rows, dtype=jnp.int32)
    key_pos = jnp.arange(seq_total, dtype=jnp.int32)
    visible = query_pos[:, None] >= key_pos[None, :]

    scores = (
        jnp.einsum("thd,uhd->htu", q_heads, k_heads, preferred_element_type=jnp.float32)
        * score_scale
    )
    row_top = jnp.max(jnp.where(visible, scores, -jnp.inf), -1, keepdims=True)
    raw = jnp.where(visible, jnp.exp(scores - row_top), 0.0)
    row_total = jnp.sum(raw, -1, keepdims=True)
    probs = raw / row_total
    probs_low = probs.astype(jnp.bfloat16)
    attended = jnp.einsum("htu,uhd->thd", probs_low, v_heads, preferred_element_type=jnp.float32)
    attended = attended.astype(jnp.bfloat16).reshape(chip_rows, half_channels)
    attn_out = from_chip_rows(attended)

    out_pad = padded(attn_out, half_width)
    conv_sum = jnp.zeros((tok_rows, channels), jnp.float32)
    filter_rows = []
    local_gf = local_g.astype(jnp.float32)
    for tap_index in range(TAPS):
        moved = out_pad[tap_index : tap_index + tok_rows].astype(jnp.float32)
        conv_sum = conv_sum + filter_taps[tap_index] * moved
        filter_rows.append(jnp.sum(moved * local_gf, 0))
    filter_gradient = butterfly_sum(jnp.stack(filter_rows, 0))
    conv_output = conv_sum.astype(jnp.bfloat16)

    dprob = jnp.einsum("thd,uhd->htu", d_heads, v_heads, preferred_element_type=jnp.float32)
    row_delta = jnp.sum(probs * dprob, -1, keepdims=True)
    dscore = (probs * (dprob - row_delta) * score_scale).astype(jnp.bfloat16)
    grad_q = jnp.einsum("htu,uhd->thd", dscore, k_heads, preferred_element_type=jnp.float32)
    grad_q = grad_q.astype(jnp.bfloat16).reshape(chip_rows, half_channels)
    key_term = jnp.einsum("htu,thd->uhd", dscore, q_heads, preferred_element_type=jnp.float32)
    value_term = jnp.einsum("htu,thd->uhd", probs_low, d_heads, preferred_element_type=jnp.float32)
    kv_terms = jnp.concatenate(
        [
            key_term.astype(jnp.bfloat16).reshape(seq_total, half_channels),
            value_term.astype(jnp.bfloat16).reshape(seq_total, half_channels),
        ],
        axis=1,
    )
    kv_grads = lax.psum_scatter(kv_terms, "sc", scatter_dimension=0, tiled=True)
    back = jnp.stack(
        [grad_q, kv_grads[:, :half_channels], kv_grads[:, half_channels:]], 0
    ).reshape(3, 2, tok_rows, 1, half_channels)
    back = lax.all_to_all(back, "core", 1, 3, tiled=True).reshape(3, tok_rows, channels)
    return (
        conv_output[None],
        back[0][None],
        back[1][None],
        back[2][None],
        filter_gradient,
    )


def solution(mesh):
    devices = np.asarray(mesh.devices)
    dp_size, seq_size = devices.shape
    split_mesh = Mesh(devices.reshape(dp_size, seq_size // 2, 2), ("dp", "sc", "core"))
    block = P("dp", SEQ, None)
    in_specs = (block, block, block, block, P())
    out_specs = (block, block, block, block, P())
    return jax.shard_map(
        on_device, mesh=split_mesh, in_specs=in_specs, out_specs=out_specs, check_vma=False
    )
```

```python
import jax
import jax.numpy as jnp
from jax import lax
from jax.sharding import PartitionSpec as P

HD = 128
TAPS = 7


def padded(value, width):
    peers = lax.axis_size("seq")
    length = value.shape[0]
    up = [(i, (i + 1) % peers) for i in range(peers)]
    down = [(j, i) for i, j in up]
    before = lax.ppermute(value[length - width :], "seq", up)
    after = lax.ppermute(value[:width], "seq", down)
    return jnp.concatenate([before, value, after], axis=0)


def butterfly_sum(value):
    axes = ("dp", "seq")
    peers = lax.axis_size("dp") * lax.axis_size("seq")
    bit = 1
    while bit < peers:
        pairs = [(i, i ^ bit) for i in range(peers)]
        value = value + lax.ppermute(value, axes, pairs)
        bit *= 2
    return value


def on_device(queries, key_states, value_states, cotangent, filter_taps):
    tok_rows = queries.shape[1]
    channels = queries.shape[2]
    seq_total = tok_rows * lax.axis_size("seq")
    head_count = channels // HD
    score_scale = HD ** (-0.5)
    half_width = (TAPS - 1) // 2
    local_q = queries[0]
    local_k = key_states[0]
    local_v = value_states[0]
    local_g = cotangent[0]
    grad_pad = padded(local_g, half_width)
    grad_sum = jnp.zeros((tok_rows, channels), jnp.float32)
    for tap_index in range(TAPS):
        start_row = 2 * half_width - tap_index
        grad_sum = grad_sum + filter_taps[tap_index] * grad_pad[
            start_row : start_row + tok_rows
        ].astype(jnp.float32)
    grad_attn = grad_sum.astype(jnp.bfloat16)

    key_all = lax.all_gather(local_k, "seq", axis=0, tiled=True)
    value_all = lax.all_gather(local_v, "seq", axis=0, tiled=True)
    q_heads = local_q.reshape(tok_rows, head_count, HD)
    d_heads = grad_attn.reshape(tok_rows, head_count, HD)
    k_heads = key_all.reshape(seq_total, head_count, HD)
    v_heads = value_all.reshape(seq_total, head_count, HD)

    device_index = lax.axis_index("seq")
    query_pos = device_index * tok_rows + jnp.arange(tok_rows, dtype=jnp.int32)
    key_pos = jnp.arange(seq_total, dtype=jnp.int32)
    visible = query_pos[:, None] >= key_pos[None, :]

    scores = (
        jnp.einsum("thd,uhd->htu", q_heads, k_heads, preferred_element_type=jnp.float32)
        * score_scale
    )
    row_top = jnp.max(jnp.where(visible, scores, -jnp.inf), -1, keepdims=True)
    raw = jnp.where(visible, jnp.exp(scores - row_top), 0.0)
    row_total = jnp.sum(raw, -1, keepdims=True)
    probs = raw / row_total
    probs_low = probs.astype(jnp.bfloat16)
    attended = jnp.einsum("htu,uhd->thd", probs_low, v_heads, preferred_element_type=jnp.float32)
    attn_out = attended.astype(jnp.bfloat16).reshape(tok_rows, channels)

    out_pad = padded(attn_out, half_width)
    conv_sum = jnp.zeros((tok_rows, channels), jnp.float32)
    filter_rows = []
    local_gf = local_g.astype(jnp.float32)
    for tap_index in range(TAPS):
        moved = out_pad[tap_index : tap_index + tok_rows].astype(jnp.float32)
        conv_sum = conv_sum + filter_taps[tap_index] * moved
        filter_rows.append(jnp.sum(moved * local_gf, 0))
    filter_gradient = butterfly_sum(jnp.stack(filter_rows, 0))
    conv_output = conv_sum.astype(jnp.bfloat16)

    value_term = jnp.einsum("htu,thd->uhd", probs_low, d_heads, preferred_element_type=jnp.float32)
    grad_values = lax.psum_scatter(
        value_term.astype(jnp.bfloat16).reshape(seq_total, channels),
        "seq", scatter_dimension=0, tiled=True,
    )
    dprob = jnp.einsum("thd,uhd->htu", d_heads, v_heads, preferred_element_type=jnp.float32)
    row_delta = jnp.sum(probs * dprob, -1, keepdims=True)
    dscore = (probs * (dprob - row_delta) * score_scale).astype(jnp.bfloat16)
    key_term = jnp.einsum("htu,thd->uhd", dscore, q_heads, preferred_element_type=jnp.float32)
    grad_keys = lax.psum_scatter(
        key_term.astype(jnp.bfloat16).reshape(seq_total, channels),
        "seq", scatter_dimension=0, tiled=True,
    )
    grad_q = jnp.einsum("htu,uhd->thd", dscore, k_heads, preferred_element_type=jnp.float32)
    grad_queries = grad_q.astype(jnp.bfloat16).reshape(tok_rows, channels)
    return (
        conv_output[None],
        grad_queries[None],
        grad_keys[None],
        grad_values[None],
        filter_gradient,
    )


def solution(mesh):
    block = P("dp", "seq", None)
    in_specs = (block, block, block, block, P())
    out_specs = (block, block, block, block, P())
    return jax.shard_map(
        on_device, mesh=mesh, in_specs=in_specs, out_specs=out_specs, check_vma=False
    )
```

```python
import jax
import jax.numpy as jnp
from jax import lax
from jax.sharding import PartitionSpec as P

HD = 128
TAPS = 7


def padded(value, width):
    peers = lax.axis_size("seq")
    length = value.shape[0]
    up = [(i, (i + 1) % peers) for i in range(peers)]
    down = [(j, i) for i, j in up]
    before = lax.ppermute(value[length - width :], "seq", up)
    after = lax.ppermute(value[:width], "seq", down)
    return jnp.concatenate([before, value, after], axis=0)


def butterfly_sum(value):
    axes = ("dp", "seq")
    peers = lax.axis_size("dp") * lax.axis_size("seq")
    bit = 1
    while bit < peers:
        pairs = [(i, i ^ bit) for i in range(peers)]
        value = value + lax.ppermute(value, axes, pairs)
        bit *= 2
    return value


def on_device(queries, key_states, value_states, cotangent, filter_taps):
    tok_rows = queries.shape[1]
    channels = queries.shape[2]
    seq_total = tok_rows * lax.axis_size("seq")
    head_count = channels // HD
    score_scale = HD ** (-0.5)
    half_width = (TAPS - 1) // 2
    local_q = queries[0]
    local_k = key_states[0]
    local_v = value_states[0]
    local_g = cotangent[0]
    grad_pad = padded(local_g, half_width)
    grad_sum = jnp.zeros((tok_rows, channels), jnp.float32)
    for tap_index in range(TAPS):
        start_row = 2 * half_width - tap_index
        grad_sum = grad_sum + filter_taps[tap_index] * grad_pad[
            start_row : start_row + tok_rows
        ].astype(jnp.float32)
    grad_attn = grad_sum.astype(jnp.bfloat16)

    key_all = lax.all_gather(local_k, "seq", axis=0, tiled=True)
    key_all, local_v = lax.optimization_barrier((key_all, local_v))
    value_all = lax.all_gather(local_v, "seq", axis=0, tiled=True)
    q_heads = local_q.reshape(tok_rows, head_count, HD)
    d_heads = grad_attn.reshape(tok_rows, head_count, HD)
    k_heads = key_all.reshape(seq_total, head_count, HD)
    v_heads = value_all.reshape(seq_total, head_count, HD)

    device_index = lax.axis_index("seq")
    query_pos = device_index * tok_rows + jnp.arange(tok_rows, dtype=jnp.int32)
    key_pos = jnp.arange(seq_total, dtype=jnp.int32)
    visible = query_pos[:, None] >= key_pos[None, :]

    scores = (
        jnp.einsum("thd,uhd->htu", q_heads, k_heads, preferred_element_type=jnp.float32)
        * score_scale
    )
    row_top = jnp.max(jnp.where(visible, scores, -jnp.inf), -1, keepdims=True)
    raw = jnp.where(visible, jnp.exp(scores - row_top), 0.0)
    row_total = jnp.sum(raw, -1, keepdims=True)
    probs = raw / row_total
    probs_low = probs.astype(jnp.bfloat16)
    value_term = jnp.einsum("htu,thd->uhd", probs_low, d_heads, preferred_element_type=jnp.float32)
    grad_values = lax.psum_scatter(
        value_term.astype(jnp.bfloat16).reshape(seq_total, channels),
        "seq", scatter_dimension=0, tiled=True,
    )
    attended = jnp.einsum("htu,uhd->thd", probs_low, v_heads, preferred_element_type=jnp.float32)
    attn_out = attended.astype(jnp.bfloat16).reshape(tok_rows, channels)

    out_pad = padded(attn_out, half_width)
    conv_sum = jnp.zeros((tok_rows, channels), jnp.float32)
    filter_rows = []
    local_gf = local_g.astype(jnp.float32)
    for tap_index in range(TAPS):
        moved = out_pad[tap_index : tap_index + tok_rows].astype(jnp.float32)
        conv_sum = conv_sum + filter_taps[tap_index] * moved
        filter_rows.append(jnp.sum(moved * local_gf, 0))
    filter_gradient = butterfly_sum(jnp.stack(filter_rows, 0))
    conv_output = conv_sum.astype(jnp.bfloat16)

    dprob = jnp.einsum("thd,uhd->htu", d_heads, v_heads, preferred_element_type=jnp.float32)
    row_delta = jnp.sum(probs * dprob, -1, keepdims=True)
    dscore = (probs * (dprob - row_delta) * score_scale).astype(jnp.bfloat16)
    key_term = jnp.einsum("htu,thd->uhd", dscore, q_heads, preferred_element_type=jnp.float32)
    grad_keys = lax.psum_scatter(
        key_term.astype(jnp.bfloat16).reshape(seq_total, channels),
        "seq", scatter_dimension=0, tiled=True,
    )
    grad_q = jnp.einsum("htu,uhd->thd", dscore, k_heads, preferred_element_type=jnp.float32)
    grad_queries = grad_q.astype(jnp.bfloat16).reshape(tok_rows, channels)
    return (
        conv_output[None],
        grad_queries[None],
        grad_keys[None],
        grad_values[None],
        filter_gradient,
    )


def solution(mesh):
    block = P("dp", "seq", None)
    in_specs = (block, block, block, block, P())
    out_specs = (block, block, block, block, P())
    return jax.shard_map(
        on_device, mesh=mesh, in_specs=in_specs, out_specs=out_specs, check_vma=False
    )
```

```python
import jax
import jax.numpy as jnp
from jax import lax
from jax.sharding import PartitionSpec as P

HD = 128
TAPS = 7


def padded(value, width):
    peers = lax.axis_size("seq")
    length = value.shape[0]
    up = [(i, (i + 1) % peers) for i in range(peers)]
    down = [(j, i) for i, j in up]
    before = lax.ppermute(value[length - width :], "seq", up)
    after = lax.ppermute(value[:width], "seq", down)
    return jnp.concatenate([before, value, after], axis=0)


def butterfly_sum(value):
    axes = ("dp", "seq")
    peers = lax.axis_size("dp") * lax.axis_size("seq")
    bit = 1
    while bit < peers:
        pairs = [(i, i ^ bit) for i in range(peers)]
        value = value + lax.ppermute(value, axes, pairs)
        bit *= 2
    return value


def butterfly_gather(value):
    peers = lax.axis_size("seq")
    index = lax.axis_index("seq")
    bit = 1
    while bit < peers:
        pairs = [(i, i ^ bit) for i in range(peers)]
        other = lax.ppermute(value, "seq", pairs)
        upper = (index & bit) != 0
        value = jnp.where(
            upper,
            jnp.concatenate([other, value], axis=0),
            jnp.concatenate([value, other], axis=0),
        )
        bit *= 2
    return value


def on_device(queries, key_states, value_states, cotangent, filter_taps):
    tok_rows = queries.shape[1]
    channels = queries.shape[2]
    peers = lax.axis_size("seq")
    seq_total = tok_rows * peers
    head_count = channels // HD
    score_scale = HD ** (-0.5)
    half_width = (TAPS - 1) // 2
    local_q = queries[0]
    local_k = key_states[0]
    local_v = value_states[0]
    local_g = cotangent[0]
    grad_pad = padded(local_g, half_width)
    grad_sum = jnp.zeros((tok_rows, channels), jnp.float32)
    for tap_index in range(TAPS):
        start_row = 2 * half_width - tap_index
        grad_sum = grad_sum + filter_taps[tap_index] * grad_pad[
            start_row : start_row + tok_rows
        ].astype(jnp.float32)
    grad_attn = grad_sum.astype(jnp.bfloat16)

    key_all = lax.all_gather(local_k, "seq", axis=0, tiled=True)
    key_all, local_v = lax.optimization_barrier((key_all, local_v))
    value_all = lax.all_gather(local_v, "seq", axis=0, tiled=True)
    value_all, local_q2 = lax.optimization_barrier((value_all, local_q))
    query_all = lax.all_gather(local_q2, "seq", axis=0, tiled=True)
    query_all, grad_attn2 = lax.optimization_barrier((query_all, grad_attn))
    grad_all = lax.all_gather(grad_attn2, "seq", axis=0, tiled=True)

    q_heads = local_q.reshape(tok_rows, head_count, HD)
    d_heads = grad_attn.reshape(tok_rows, head_count, HD)
    k_heads = key_all.reshape(seq_total, head_count, HD)
    v_heads = value_all.reshape(seq_total, head_count, HD)

    device_index = lax.axis_index("seq")
    own_pos = device_index * tok_rows + jnp.arange(tok_rows, dtype=jnp.int32)
    all_pos = jnp.arange(seq_total, dtype=jnp.int32)
    visible = own_pos[:, None] >= all_pos[None, :]

    scores = (
        jnp.einsum("thd,uhd->htu", q_heads, k_heads, preferred_element_type=jnp.float32)
        * score_scale
    )
    row_top = jnp.max(jnp.where(visible, scores, -jnp.inf), -1, keepdims=True)
    raw = jnp.where(visible, jnp.exp(scores - row_top), 0.0)
    row_total = jnp.sum(raw, -1, keepdims=True)
    probs = raw / row_total
    probs_low = probs.astype(jnp.bfloat16)
    attended = jnp.einsum("htu,uhd->thd", probs_low, v_heads, preferred_element_type=jnp.float32)
    attn_out = attended.astype(jnp.bfloat16).reshape(tok_rows, channels)
    dprob = jnp.einsum("thd,uhd->htu", d_heads, v_heads, preferred_element_type=jnp.float32)
    row_delta = jnp.sum(probs * dprob, -1, keepdims=True)
    dscore = (probs * (dprob - row_delta) * score_scale).astype(jnp.bfloat16)
    grad_q = jnp.einsum("htu,uhd->thd", dscore, k_heads, preferred_element_type=jnp.float32)
    grad_queries = grad_q.astype(jnp.bfloat16).reshape(tok_rows, channels)

    stats = jnp.stack([row_top[..., 0], row_total[..., 0], row_delta[..., 0]], 0)
    stats = butterfly_gather(stats.transpose(2, 0, 1)).transpose(1, 0, 2)
    top_all = stats[0].T[:, None, :]
    total_all = stats[1].T[:, None, :]
    delta_all = stats[2].T[:, None, :]

    kq_heads = local_k.reshape(tok_rows, head_count, HD)
    kv_heads = local_v.reshape(tok_rows, head_count, HD)
    qa_heads = query_all.reshape(seq_total, head_count, HD)
    da_heads = grad_all.reshape(seq_total, head_count, HD)
    key_visible = all_pos[None, :] >= own_pos[:, None]
    scores_t = (
        jnp.einsum("uhd,thd->hut", kq_heads, qa_heads, preferred_element_type=jnp.float32)
        * score_scale
    )
    raw_t = jnp.where(key_visible, jnp.exp(scores_t - top_all), 0.0)
    probs_t = raw_t / total_all
    probs_low_t = probs_t.astype(jnp.bfloat16)
    dprob_t = jnp.einsum("uhd,thd->hut", kv_heads, da_heads, preferred_element_type=jnp.float32)
    dscore_t = (probs_t * (dprob_t - delta_all) * score_scale).astype(jnp.bfloat16)
    grad_k = jnp.einsum("hut,thd->uhd", dscore_t, qa_heads, preferred_element_type=jnp.float32)
    grad_v = jnp.einsum("hut,thd->uhd", probs_low_t, da_heads, preferred_element_type=jnp.float32)
    grad_keys = grad_k.astype(jnp.bfloat16).reshape(tok_rows, channels)
    grad_values = grad_v.astype(jnp.bfloat16).reshape(tok_rows, channels)

    out_pad = padded(attn_out, half_width)
    conv_sum = jnp.zeros((tok_rows, channels), jnp.float32)
    filter_rows = []
    local_gf = local_g.astype(jnp.float32)
    for tap_index in range(TAPS):
        moved = out_pad[tap_index : tap_index + tok_rows].astype(jnp.float32)
        conv_sum = conv_sum + filter_taps[tap_index] * moved
        filter_rows.append(jnp.sum(moved * local_gf, 0))
    filter_gradient = butterfly_sum(jnp.stack(filter_rows, 0))
    conv_output = conv_sum.astype(jnp.bfloat16)
    return (
        conv_output[None],
        grad_queries[None],
        grad_keys[None],
        grad_values[None],
        filter_gradient,
    )


def solution(mesh):
    block = P("dp", "seq", None)
    in_specs = (block, block, block, block, P())
    out_specs = (block, block, block, block, P())
    return jax.shard_map(
        on_device, mesh=mesh, in_specs=in_specs, out_specs=out_specs, check_vma=False
    )
```

```python
import jax
import jax.numpy as jnp
from jax import lax
from jax.sharding import PartitionSpec as P

HD = 128
TAPS = 7


def padded(value, width):
    peers = lax.axis_size("seq")
    length = value.shape[0]
    up = [(i, (i + 1) % peers) for i in range(peers)]
    down = [(j, i) for i, j in up]
    before = lax.ppermute(value[length - width :], "seq", up)
    after = lax.ppermute(value[:width], "seq", down)
    return jnp.concatenate([before, value, after], axis=0)


def butterfly_sum(value):
    axes = ("dp", "seq")
    peers = lax.axis_size("dp") * lax.axis_size("seq")
    bit = 1
    while bit < peers:
        pairs = [(i, i ^ bit) for i in range(peers)]
        value = value + lax.ppermute(value, axes, pairs)
        bit *= 2
    return value


def butterfly_gather(value):
    peers = lax.axis_size("seq")
    index = lax.axis_index("seq")
    bit = 1
    while bit < peers:
        pairs = [(i, i ^ bit) for i in range(peers)]
        other = lax.ppermute(value, "seq", pairs)
        upper = (index & bit) != 0
        value = jnp.where(
            upper,
            jnp.concatenate([other, value], axis=0),
            jnp.concatenate([value, other], axis=0),
        )
        bit *= 2
    return value


def on_device(queries, key_states, value_states, cotangent, filter_taps):
    tok_rows = queries.shape[1]
    channels = queries.shape[2]
    peers = lax.axis_size("seq")
    seq_total = tok_rows * peers
    head_count = channels // HD
    score_scale = HD ** (-0.5)
    half_width = (TAPS - 1) // 2
    local_q = queries[0]
    local_k = key_states[0]
    local_v = value_states[0]
    local_g = cotangent[0]
    grad_pad = padded(local_g, half_width)
    grad_sum = jnp.zeros((tok_rows, channels), jnp.float32)
    for tap_index in range(TAPS):
        start_row = 2 * half_width - tap_index
        grad_sum = grad_sum + filter_taps[tap_index] * grad_pad[
            start_row : start_row + tok_rows
        ].astype(jnp.float32)
    grad_attn = grad_sum.astype(jnp.bfloat16)

    key_all = lax.all_gather(local_k, "seq", axis=0, tiled=True)
    key_all, local_v = lax.optimization_barrier((key_all, local_v))
    value_all = lax.all_gather(local_v, "seq", axis=0, tiled=True)

    q_heads = local_q.reshape(tok_rows, head_count, HD)
    d_heads = grad_attn.reshape(tok_rows, head_count, HD)
    k_heads = key_all.reshape(seq_total, head_count, HD)
    v_heads = value_all.reshape(seq_total, head_count, HD)

    device_index = lax.axis_index("seq")
    own_pos = device_index * tok_rows + jnp.arange(tok_rows, dtype=jnp.int32)
    all_pos = jnp.arange(seq_total, dtype=jnp.int32)
    visible = own_pos[:, None] >= all_pos[None, :]

    scores = (
        jnp.einsum("thd,uhd->htu", q_heads, k_heads, preferred_element_type=jnp.float32)
        * score_scale
    )
    row_top = jnp.max(jnp.where(visible, scores, -jnp.inf), -1, keepdims=True)
    raw = jnp.where(visible, jnp.exp(scores - row_top), 0.0)
    row_total = jnp.sum(raw, -1, keepdims=True)
    probs = raw / row_total
    probs_low = probs.astype(jnp.bfloat16)
    probs_low, local_q2 = lax.optimization_barrier((probs_low, local_q))
    query_all = lax.all_gather(local_q2, "seq", axis=0, tiled=True)
    attended = jnp.einsum("htu,uhd->thd", probs_low, v_heads, preferred_element_type=jnp.float32)
    attn_out = attended.astype(jnp.bfloat16).reshape(tok_rows, channels)
    dprob = jnp.einsum("thd,uhd->htu", d_heads, v_heads, preferred_element_type=jnp.float32)
    row_delta = jnp.sum(probs * dprob, -1, keepdims=True)
    dscore = (probs * (dprob - row_delta) * score_scale).astype(jnp.bfloat16)
    dscore, grad_attn2 = lax.optimization_barrier((dscore, grad_attn))
    grad_all = lax.all_gather(grad_attn2, "seq", axis=0, tiled=True)
    grad_q = jnp.einsum("htu,uhd->thd", dscore, k_heads, preferred_element_type=jnp.float32)
    grad_queries = grad_q.astype(jnp.bfloat16).reshape(tok_rows, channels)

    stats = jnp.stack([row_top[..., 0], row_total[..., 0], row_delta[..., 0]], 0)
    stats = butterfly_gather(stats.transpose(2, 0, 1)).transpose(1, 0, 2)
    top_all = stats[0].T[:, None, :]
    total_all = stats[1].T[:, None, :]
    delta_all = stats[2].T[:, None, :]

    kq_heads = local_k.reshape(tok_rows, head_count, HD)
    kv_heads = local_v.reshape(tok_rows, head_count, HD)
    qa_heads = query_all.reshape(seq_total, head_count, HD)
    da_heads = grad_all.reshape(seq_total, head_count, HD)
    key_visible = all_pos[None, :] >= own_pos[:, None]
    scores_t = (
        jnp.einsum("uhd,thd->hut", kq_heads, qa_heads, preferred_element_type=jnp.float32)
        * score_scale
    )
    raw_t = jnp.where(key_visible, jnp.exp(scores_t - top_all), 0.0)
    probs_t = raw_t / total_all
    probs_low_t = probs_t.astype(jnp.bfloat16)
    dprob_t = jnp.einsum("uhd,thd->hut", kv_heads, da_heads, preferred_element_type=jnp.float32)
    dscore_t = (probs_t * (dprob_t - delta_all) * score_scale).astype(jnp.bfloat16)
    grad_k = jnp.einsum("hut,thd->uhd", dscore_t, qa_heads, preferred_element_type=jnp.float32)
    grad_v = jnp.einsum("hut,thd->uhd", probs_low_t, da_heads, preferred_element_type=jnp.float32)
    grad_keys = grad_k.astype(jnp.bfloat16).reshape(tok_rows, channels)
    grad_values = grad_v.astype(jnp.bfloat16).reshape(tok_rows, channels)

    out_pad = padded(attn_out, half_width)
    conv_sum = jnp.zeros((tok_rows, channels), jnp.float32)
    filter_rows = []
    local_gf = local_g.astype(jnp.float32)
    for tap_index in range(TAPS):
        moved = out_pad[tap_index : tap_index + tok_rows].astype(jnp.float32)
        conv_sum = conv_sum + filter_taps[tap_index] * moved
        filter_rows.append(jnp.sum(moved * local_gf, 0))
    filter_gradient = butterfly_sum(jnp.stack(filter_rows, 0))
    conv_output = conv_sum.astype(jnp.bfloat16)
    return (
        conv_output[None],
        grad_queries[None],
        grad_keys[None],
        grad_values[None],
        filter_gradient,
    )


def solution(mesh):
    block = P("dp", "seq", None)
    in_specs = (block, block, block, block, P())
    out_specs = (block, block, block, block, P())
    return jax.shard_map(
        on_device, mesh=mesh, in_specs=in_specs, out_specs=out_specs, check_vma=False
    )
```

```python
import jax
import jax.numpy as jnp
from jax import lax
from jax.sharding import PartitionSpec as P

HD = 128
TAPS = 7


def padded(value, width):
    peers = lax.axis_size("seq")
    length = value.shape[0]
    up = [(i, (i + 1) % peers) for i in range(peers)]
    down = [(j, i) for i, j in up]
    before = lax.ppermute(value[length - width :], "seq", up)
    after = lax.ppermute(value[:width], "seq", down)
    return jnp.concatenate([before, value, after], axis=0)


def butterfly_sum(value):
    axes = ("dp", "seq")
    peers = lax.axis_size("dp") * lax.axis_size("seq")
    bit = 1
    while bit < peers:
        pairs = [(i, i ^ bit) for i in range(peers)]
        value = value + lax.ppermute(value, axes, pairs)
        bit *= 2
    return value


def butterfly_gather(value):
    peers = lax.axis_size("seq")
    index = lax.axis_index("seq")
    bit = 1
    while bit < peers:
        pairs = [(i, i ^ bit) for i in range(peers)]
        other = lax.ppermute(value, "seq", pairs)
        upper = (index & bit) != 0
        value = jnp.where(
            upper,
            jnp.concatenate([other, value], axis=0),
            jnp.concatenate([value, other], axis=0),
        )
        bit *= 2
    return value


def on_device(queries, key_states, value_states, cotangent, filter_taps):
    tok_rows = queries.shape[1]
    channels = queries.shape[2]
    peers = lax.axis_size("seq")
    seq_total = tok_rows * peers
    head_count = channels // HD
    score_scale = HD ** (-0.5)
    half_width = (TAPS - 1) // 2
    local_q = queries[0]
    local_k = key_states[0]
    local_v = value_states[0]
    local_g = cotangent[0]
    grad_pad = padded(local_g, half_width)
    grad_sum = jnp.zeros((tok_rows, channels), jnp.float32)
    for tap_index in range(TAPS):
        start_row = 2 * half_width - tap_index
        grad_sum = grad_sum + filter_taps[tap_index] * grad_pad[
            start_row : start_row + tok_rows
        ].astype(jnp.float32)
    grad_attn = grad_sum.astype(jnp.bfloat16)

    key_all = lax.all_gather(local_k, "seq", axis=0, tiled=True)
    key_all, local_v = lax.optimization_barrier((key_all, local_v))
    value_all = lax.all_gather(local_v, "seq", axis=0, tiled=True)

    q_heads = local_q.reshape(tok_rows, head_count, HD)
    d_heads = grad_attn.reshape(tok_rows, head_count, HD)
    k_heads = key_all.reshape(seq_total, head_count, HD)
    v_heads = value_all.reshape(seq_total, head_count, HD)

    device_index = lax.axis_index("seq")
    own_pos = device_index * tok_rows + jnp.arange(tok_rows, dtype=jnp.int32)
    all_pos = jnp.arange(seq_total, dtype=jnp.int32)
    visible = own_pos[:, None] >= all_pos[None, :]

    scores = (
        jnp.einsum("thd,uhd->htu", q_heads, k_heads, preferred_element_type=jnp.float32)
        * score_scale
    )
    row_top = jnp.max(jnp.where(visible, scores, -jnp.inf), -1, keepdims=True)
    row_top, local_q2 = lax.optimization_barrier((row_top, local_q))
    query_all = lax.all_gather(local_q2, "seq", axis=0, tiled=True)
    raw = jnp.where(visible, jnp.exp(scores - row_top), 0.0)
    row_total = jnp.sum(raw, -1, keepdims=True)
    probs = raw / row_total
    probs_low = probs.astype(jnp.bfloat16)
    probs_low, grad_attn2 = lax.optimization_barrier((probs_low, grad_attn))
    grad_all = lax.all_gather(grad_attn2, "seq", axis=0, tiled=True)
    attended = jnp.einsum("htu,uhd->thd", probs_low, v_heads, preferred_element_type=jnp.float32)
    attn_out = attended.astype(jnp.bfloat16).reshape(tok_rows, channels)
    dprob = jnp.einsum("thd,uhd->htu", d_heads, v_heads, preferred_element_type=jnp.float32)
    row_delta = jnp.sum(probs * dprob, -1, keepdims=True)
    dscore = (probs * (dprob - row_delta) * score_scale).astype(jnp.bfloat16)
    grad_q = jnp.einsum("htu,uhd->thd", dscore, k_heads, preferred_element_type=jnp.float32)
    grad_queries = grad_q.astype(jnp.bfloat16).reshape(tok_rows, channels)

    stats = jnp.stack([row_top[..., 0], row_total[..., 0], row_delta[..., 0]], 0)
    stats = butterfly_gather(stats.transpose(2, 0, 1)).transpose(1, 0, 2)
    top_all = stats[0].T[:, None, :]
    total_all = stats[1].T[:, None, :]
    delta_all = stats[2].T[:, None, :]

    kq_heads = local_k.reshape(tok_rows, head_count, HD)
    kv_heads = local_v.reshape(tok_rows, head_count, HD)
    qa_heads = query_all.reshape(seq_total, head_count, HD)
    da_heads = grad_all.reshape(seq_total, head_count, HD)
    key_visible = all_pos[None, :] >= own_pos[:, None]
    scores_t = (
        jnp.einsum("uhd,thd->hut", kq_heads, qa_heads, preferred_element_type=jnp.float32)
        * score_scale
    )
    raw_t = jnp.where(key_visible, jnp.exp(scores_t - top_all), 0.0)
    probs_t = raw_t / total_all
    probs_low_t = probs_t.astype(jnp.bfloat16)
    dprob_t = jnp.einsum("uhd,thd->hut", kv_heads, da_heads, preferred_element_type=jnp.float32)
    dscore_t = (probs_t * (dprob_t - delta_all) * score_scale).astype(jnp.bfloat16)
    grad_k = jnp.einsum("hut,thd->uhd", dscore_t, qa_heads, preferred_element_type=jnp.float32)
    grad_v = jnp.einsum("hut,thd->uhd", probs_low_t, da_heads, preferred_element_type=jnp.float32)
    grad_keys = grad_k.astype(jnp.bfloat16).reshape(tok_rows, channels)
    grad_values = grad_v.astype(jnp.bfloat16).reshape(tok_rows, channels)

    out_pad = padded(attn_out, half_width)
    conv_sum = jnp.zeros((tok_rows, channels), jnp.float32)
    filter_rows = []
    local_gf = local_g.astype(jnp.float32)
    for tap_index in range(TAPS):
        moved = out_pad[tap_index : tap_index + tok_rows].astype(jnp.float32)
        conv_sum = conv_sum + filter_taps[tap_index] * moved
        filter_rows.append(jnp.sum(moved * local_gf, 0))
    filter_gradient = butterfly_sum(jnp.stack(filter_rows, 0))
    conv_output = conv_sum.astype(jnp.bfloat16)
    return (
        conv_output[None],
        grad_queries[None],
        grad_keys[None],
        grad_values[None],
        filter_gradient,
    )


def solution(mesh):
    block = P("dp", "seq", None)
    in_specs = (block, block, block, block, P())
    out_specs = (block, block, block, block, P())
    return jax.shard_map(
        on_device, mesh=mesh, in_specs=in_specs, out_specs=out_specs, check_vma=False
    )
```

```python
import jax
import jax.numpy as jnp
from jax import lax
from jax.sharding import PartitionSpec as P

HD = 128
TAPS = 7


def padded(value, width):
    peers = lax.axis_size("seq")
    length = value.shape[0]
    up = [(i, (i + 1) % peers) for i in range(peers)]
    down = [(j, i) for i, j in up]
    before = lax.ppermute(value[length - width :], "seq", up)
    after = lax.ppermute(value[:width], "seq", down)
    return jnp.concatenate([before, value, after], axis=0)


def butterfly_sum(value):
    axes = ("dp", "seq")
    peers = lax.axis_size("dp") * lax.axis_size("seq")
    bit = 1
    while bit < peers:
        pairs = [(i, i ^ bit) for i in range(peers)]
        value = value + lax.ppermute(value, axes, pairs)
        bit *= 2
    return value


def butterfly_gather(value):
    peers = lax.axis_size("seq")
    index = lax.axis_index("seq")
    bit = 1
    while bit < peers:
        pairs = [(i, i ^ bit) for i in range(peers)]
        other = lax.ppermute(value, "seq", pairs)
        upper = (index & bit) != 0
        value = jnp.where(
            upper,
            jnp.concatenate([other, value], axis=0),
            jnp.concatenate([value, other], axis=0),
        )
        bit *= 2
    return value


def on_device(queries, key_states, value_states, cotangent, filter_taps):
    tok_rows = queries.shape[1]
    channels = queries.shape[2]
    peers = lax.axis_size("seq")
    seq_total = tok_rows * peers
    head_count = channels // HD
    score_scale = HD ** (-0.5)
    half_width = (TAPS - 1) // 2
    local_q = queries[0]
    local_k = key_states[0]
    local_v = value_states[0]
    local_g = cotangent[0]
    grad_pad = padded(local_g, half_width)
    grad_sum = jnp.zeros((tok_rows, channels), jnp.float32)
    for tap_index in range(TAPS):
        start_row = 2 * half_width - tap_index
        grad_sum = grad_sum + filter_taps[tap_index] * grad_pad[
            start_row : start_row + tok_rows
        ].astype(jnp.float32)
    grad_attn = grad_sum.astype(jnp.bfloat16)

    kv_all = lax.all_gather(
        jnp.concatenate([local_k, local_v], axis=1), "seq", axis=0, tiled=True
    )
    key_all = kv_all[:, :channels]
    value_all = kv_all[:, channels:]

    q_heads = local_q.reshape(tok_rows, head_count, HD)
    d_heads = grad_attn.reshape(tok_rows, head_count, HD)
    k_heads = key_all.reshape(seq_total, head_count, HD)
    v_heads = value_all.reshape(seq_total, head_count, HD)

    device_index = lax.axis_index("seq")
    own_pos = device_index * tok_rows + jnp.arange(tok_rows, dtype=jnp.int32)
    all_pos = jnp.arange(seq_total, dtype=jnp.int32)
    visible = own_pos[:, None] >= all_pos[None, :]

    scores = (
        jnp.einsum("thd,uhd->htu", q_heads, k_heads, preferred_element_type=jnp.float32)
        * score_scale
    )
    row_top = jnp.max(jnp.where(visible, scores, -jnp.inf), -1, keepdims=True)
    row_top, local_q2 = lax.optimization_barrier((row_top, local_q))
    query_all = lax.all_gather(local_q2, "seq", axis=0, tiled=True)
    raw = jnp.where(visible, jnp.exp(scores - row_top), 0.0)
    row_total = jnp.sum(raw, -1, keepdims=True)
    probs = raw / row_total
    probs_low = probs.astype(jnp.bfloat16)
    probs_low, grad_attn2 = lax.optimization_barrier((probs_low, grad_attn))
    grad_all = lax.all_gather(grad_attn2, "seq", axis=0, tiled=True)
    attended = jnp.einsum("htu,uhd->thd", probs_low, v_heads, preferred_element_type=jnp.float32)
    attn_out = attended.astype(jnp.bfloat16).reshape(tok_rows, channels)
    dprob = jnp.einsum("thd,uhd->htu", d_heads, v_heads, preferred_element_type=jnp.float32)
    row_delta = jnp.sum(probs * dprob, -1, keepdims=True)
    dscore = (probs * (dprob - row_delta) * score_scale).astype(jnp.bfloat16)
    grad_q = jnp.einsum("htu,uhd->thd", dscore, k_heads, preferred_element_type=jnp.float32)
    grad_queries = grad_q.astype(jnp.bfloat16).reshape(tok_rows, channels)

    stats = jnp.stack([row_top[..., 0], row_total[..., 0], row_delta[..., 0]], 0)
    stats = butterfly_gather(stats.transpose(2, 0, 1)).transpose(1, 0, 2)
    top_all = stats[0].T[:, None, :]
    total_all = stats[1].T[:, None, :]
    delta_all = stats[2].T[:, None, :]

    kq_heads = local_k.reshape(tok_rows, head_count, HD)
    kv_heads = local_v.reshape(tok_rows, head_count, HD)
    qa_heads = query_all.reshape(seq_total, head_count, HD)
    da_heads = grad_all.reshape(seq_total, head_count, HD)
    key_visible = all_pos[None, :] >= own_pos[:, None]
    scores_t = (
        jnp.einsum("uhd,thd->hut", kq_heads, qa_heads, preferred_element_type=jnp.float32)
        * score_scale
    )
    raw_t = jnp.where(key_visible, jnp.exp(scores_t - top_all), 0.0)
    probs_t = raw_t / total_all
    probs_low_t = probs_t.astype(jnp.bfloat16)
    dprob_t = jnp.einsum("uhd,thd->hut", kv_heads, da_heads, preferred_element_type=jnp.float32)
    dscore_t = (probs_t * (dprob_t - delta_all) * score_scale).astype(jnp.bfloat16)
    grad_k = jnp.einsum("hut,thd->uhd", dscore_t, qa_heads, preferred_element_type=jnp.float32)
    grad_v = jnp.einsum("hut,thd->uhd", probs_low_t, da_heads, preferred_element_type=jnp.float32)
    grad_keys = grad_k.astype(jnp.bfloat16).reshape(tok_rows, channels)
    grad_values = grad_v.astype(jnp.bfloat16).reshape(tok_rows, channels)

    out_pad = padded(attn_out, half_width)
    conv_sum = jnp.zeros((tok_rows, channels), jnp.float32)
    filter_rows = []
    local_gf = local_g.astype(jnp.float32)
    for tap_index in range(TAPS):
        moved = out_pad[tap_index : tap_index + tok_rows].astype(jnp.float32)
        conv_sum = conv_sum + filter_taps[tap_index] * moved
        filter_rows.append(jnp.sum(moved * local_gf, 0))
    filter_gradient = butterfly_sum(jnp.stack(filter_rows, 0))
    conv_output = conv_sum.astype(jnp.bfloat16)
    return (
        conv_output[None],
        grad_queries[None],
        grad_keys[None],
        grad_values[None],
        filter_gradient,
    )


def solution(mesh):
    block = P("dp", "seq", None)
    in_specs = (block, block, block, block, P())
    out_specs = (block, block, block, block, P())
    return jax.shard_map(
        on_device, mesh=mesh, in_specs=in_specs, out_specs=out_specs, check_vma=False
    )
```

```python
import jax
import jax.numpy as jnp
from jax import lax
from jax.sharding import PartitionSpec as P

HD = 128
TAPS = 7


def padded(value, width):
    peers = lax.axis_size("seq")
    length = value.shape[0]
    up = [(i, (i + 1) % peers) for i in range(peers)]
    down = [(j, i) for i, j in up]
    before = lax.ppermute(value[length - width :], "seq", up)
    after = lax.ppermute(value[:width], "seq", down)
    return jnp.concatenate([before, value, after], axis=0)


def butterfly_sum(value):
    axes = ("dp", "seq")
    peers = lax.axis_size("dp") * lax.axis_size("seq")
    bit = 1
    while bit < peers:
        pairs = [(i, i ^ bit) for i in range(peers)]
        value = value + lax.ppermute(value, axes, pairs)
        bit *= 2
    return value


def butterfly_gather(value):
    peers = lax.axis_size("seq")
    index = lax.axis_index("seq")
    bit = 1
    while bit < peers:
        pairs = [(i, i ^ bit) for i in range(peers)]
        other = lax.ppermute(value, "seq", pairs)
        upper = (index & bit) != 0
        value = jnp.where(
            upper,
            jnp.concatenate([other, value], axis=0),
            jnp.concatenate([value, other], axis=0),
        )
        bit *= 2
    return value


def on_device(queries, key_states, value_states, cotangent, filter_taps):
    tok_rows = queries.shape[1]
    channels = queries.shape[2]
    peers = lax.axis_size("seq")
    seq_total = tok_rows * peers
    head_count = channels // HD
    score_scale = HD ** (-0.5)
    half_width = (TAPS - 1) // 2
    local_q = queries[0]
    local_k = key_states[0]
    local_v = value_states[0]
    local_g = cotangent[0]
    grad_pad = padded(local_g, half_width)
    grad_sum = jnp.zeros((tok_rows, channels), jnp.float32)
    for tap_index in range(TAPS):
        start_row = 2 * half_width - tap_index
        grad_sum = grad_sum + filter_taps[tap_index] * grad_pad[
            start_row : start_row + tok_rows
        ].astype(jnp.float32)
    grad_attn = grad_sum.astype(jnp.bfloat16)

    def head_major(matrix):
        return matrix.reshape(tok_rows, head_count, HD).transpose(1, 0, 2)

    k_heads = lax.all_gather(head_major(local_k), "seq", axis=1, tiled=True)
    k_heads, local_v = lax.optimization_barrier((k_heads, local_v))
    v_heads = lax.all_gather(head_major(local_v), "seq", axis=1, tiled=True)

    q_heads = local_q.reshape(tok_rows, head_count, HD)
    d_heads = grad_attn.reshape(tok_rows, head_count, HD)

    device_index = lax.axis_index("seq")
    own_pos = device_index * tok_rows + jnp.arange(tok_rows, dtype=jnp.int32)
    all_pos = jnp.arange(seq_total, dtype=jnp.int32)
    visible = own_pos[:, None] >= all_pos[None, :]

    scores = (
        jnp.einsum("thd,hud->htu", q_heads, k_heads, preferred_element_type=jnp.float32)
        * score_scale
    )
    row_top = jnp.max(jnp.where(visible, scores, -jnp.inf), -1, keepdims=True)
    row_top, local_q2 = lax.optimization_barrier((row_top, local_q))
    qa_heads = lax.all_gather(head_major(local_q2), "seq", axis=1, tiled=True)
    raw = jnp.where(visible, jnp.exp(scores - row_top), 0.0)
    row_total = jnp.sum(raw, -1, keepdims=True)
    probs = raw / row_total
    probs_low = probs.astype(jnp.bfloat16)
    probs_low, grad_attn2 = lax.optimization_barrier((probs_low, grad_attn))
    da_heads = lax.all_gather(head_major(grad_attn2), "seq", axis=1, tiled=True)
    attended = jnp.einsum("htu,hud->thd", probs_low, v_heads, preferred_element_type=jnp.float32)
    attn_out = attended.astype(jnp.bfloat16).reshape(tok_rows, channels)
    dprob = jnp.einsum("thd,hud->htu", d_heads, v_heads, preferred_element_type=jnp.float32)
    row_delta = jnp.sum(probs * dprob, -1, keepdims=True)
    dscore = (probs * (dprob - row_delta) * score_scale).astype(jnp.bfloat16)
    grad_q = jnp.einsum("htu,hud->thd", dscore, k_heads, preferred_element_type=jnp.float32)
    grad_queries = grad_q.astype(jnp.bfloat16).reshape(tok_rows, channels)

    stats = jnp.stack([row_top[..., 0], row_total[..., 0], row_delta[..., 0]], 0)
    stats = butterfly_gather(stats.transpose(2, 0, 1)).transpose(1, 0, 2)
    top_all = stats[0].T[:, None, :]
    total_all = stats[1].T[:, None, :]
    delta_all = stats[2].T[:, None, :]

    kq_heads = local_k.reshape(tok_rows, head_count, HD)
    kv_heads = local_v.reshape(tok_rows, head_count, HD)
    key_visible = all_pos[None, :] >= own_pos[:, None]
    scores_t = (
        jnp.einsum("uhd,htd->hut", kq_heads, qa_heads, preferred_element_type=jnp.float32)
        * score_scale
    )
    raw_t = jnp.where(key_visible, jnp.exp(scores_t - top_all), 0.0)
    probs_t = raw_t / total_all
    probs_low_t = probs_t.astype(jnp.bfloat16)
    dprob_t = jnp.einsum("uhd,htd->hut", kv_heads, da_heads, preferred_element_type=jnp.float32)
    dscore_t = (probs_t * (dprob_t - delta_all) * score_scale).astype(jnp.bfloat16)
    grad_k = jnp.einsum("hut,htd->uhd", dscore_t, qa_heads, preferred_element_type=jnp.float32)
    grad_v = jnp.einsum("hut,htd->uhd", probs_low_t, da_heads, preferred_element_type=jnp.float32)
    grad_keys = grad_k.astype(jnp.bfloat16).reshape(tok_rows, channels)
    grad_values = grad_v.astype(jnp.bfloat16).reshape(tok_rows, channels)

    out_pad = padded(attn_out, half_width)
    conv_sum = jnp.zeros((tok_rows, channels), jnp.float32)
    filter_rows = []
    local_gf = local_g.astype(jnp.float32)
    for tap_index in range(TAPS):
        moved = out_pad[tap_index : tap_index + tok_rows].astype(jnp.float32)
        conv_sum = conv_sum + filter_taps[tap_index] * moved
        filter_rows.append(jnp.sum(moved * local_gf, 0))
    filter_gradient = butterfly_sum(jnp.stack(filter_rows, 0))
    conv_output = conv_sum.astype(jnp.bfloat16)
    return (
        conv_output[None],
        grad_queries[None],
        grad_keys[None],
        grad_values[None],
        filter_gradient,
    )


def solution(mesh):
    block = P("dp", "seq", None)
    in_specs = (block, block, block, block, P())
    out_specs = (block, block, block, block, P())
    return jax.shard_map(
        on_device, mesh=mesh, in_specs=in_specs, out_specs=out_specs, check_vma=False
    )
```

```python
import jax
import jax.numpy as jnp
from jax import lax
from jax.sharding import PartitionSpec as P

HD = 128
TAPS = 7


def padded(value, width):
    peers = lax.axis_size("seq")
    length = value.shape[0]
    up = [(i, (i + 1) % peers) for i in range(peers)]
    down = [(j, i) for i, j in up]
    before = lax.ppermute(value[length - width :], "seq", up)
    after = lax.ppermute(value[:width], "seq", down)
    return jnp.concatenate([before, value, after], axis=0)


def butterfly_sum(value):
    axes = ("dp", "seq")
    peers = lax.axis_size("dp") * lax.axis_size("seq")
    bit = 1
    while bit < peers:
        pairs = [(i, i ^ bit) for i in range(peers)]
        value = value + lax.ppermute(value, axes, pairs)
        bit *= 2
    return value


def butterfly_gather(value):
    peers = lax.axis_size("seq")
    index = lax.axis_index("seq")
    bit = 1
    while bit < peers:
        pairs = [(i, i ^ bit) for i in range(peers)]
        other = lax.ppermute(value, "seq", pairs)
        upper = (index & bit) != 0
        value = jnp.where(
            upper,
            jnp.concatenate([other, value], axis=0),
            jnp.concatenate([value, other], axis=0),
        )
        bit *= 2
    return value


def on_device(queries, key_states, value_states, cotangent, filter_taps):
    tok_rows = queries.shape[1]
    channels = queries.shape[2]
    peers = lax.axis_size("seq")
    seq_total = tok_rows * peers
    head_count = channels // HD
    score_scale = HD ** (-0.5)
    half_width = (TAPS - 1) // 2
    local_q = queries[0]
    local_k = key_states[0]
    local_v = value_states[0]
    local_g = cotangent[0]
    grad_pad = padded(local_g, half_width)
    grad_sum = jnp.zeros((tok_rows, channels), jnp.float32)
    for tap_index in range(TAPS):
        start_row = 2 * half_width - tap_index
        grad_sum = grad_sum + filter_taps[tap_index] * grad_pad[
            start_row : start_row + tok_rows
        ].astype(jnp.float32)
    grad_attn = grad_sum.astype(jnp.bfloat16)

    def head_major(matrix):
        return matrix.reshape(tok_rows, head_count, HD).transpose(1, 0, 2)

    k_heads = lax.all_gather(local_k, "seq", axis=0, tiled=True).reshape(seq_total, head_count, HD)
    k_heads, local_v = lax.optimization_barrier((k_heads, local_v))
    v_heads = lax.all_gather(head_major(local_v), "seq", axis=1, tiled=True)

    q_heads = local_q.reshape(tok_rows, head_count, HD)
    d_heads = grad_attn.reshape(tok_rows, head_count, HD)

    device_index = lax.axis_index("seq")
    own_pos = device_index * tok_rows + jnp.arange(tok_rows, dtype=jnp.int32)
    all_pos = jnp.arange(seq_total, dtype=jnp.int32)
    visible = own_pos[:, None] >= all_pos[None, :]

    scores = (
        jnp.einsum("thd,uhd->htu", q_heads, k_heads, preferred_element_type=jnp.float32)
        * score_scale
    )
    row_top = jnp.max(jnp.where(visible, scores, -jnp.inf), -1, keepdims=True)
    row_top, local_q2 = lax.optimization_barrier((row_top, local_q))
    qa_heads = lax.all_gather(head_major(local_q2), "seq", axis=1, tiled=True)
    raw = jnp.where(visible, jnp.exp(scores - row_top), 0.0)
    row_total = jnp.sum(raw, -1, keepdims=True)
    probs = raw / row_total
    probs_low = probs.astype(jnp.bfloat16)
    probs_low, grad_attn2 = lax.optimization_barrier((probs_low, grad_attn))
    da_heads = lax.all_gather(head_major(grad_attn2), "seq", axis=1, tiled=True)
    attended = jnp.einsum("htu,hud->thd", probs_low, v_heads, preferred_element_type=jnp.float32)
    attn_out = attended.astype(jnp.bfloat16).reshape(tok_rows, channels)
    dprob = jnp.einsum("thd,hud->htu", d_heads, v_heads, preferred_element_type=jnp.float32)
    row_delta = jnp.sum(probs * dprob, -1, keepdims=True)
    dscore = (probs * (dprob - row_delta) * score_scale).astype(jnp.bfloat16)
    grad_q = jnp.einsum("htu,uhd->thd", dscore, k_heads, preferred_element_type=jnp.float32)
    grad_queries = grad_q.astype(jnp.bfloat16).reshape(tok_rows, channels)

    stats = jnp.stack([row_top[..., 0], row_total[..., 0], row_delta[..., 0]], 0)
    stats = butterfly_gather(stats.transpose(2, 0, 1)).transpose(1, 0, 2)
    top_all = stats[0].T[:, None, :]
    total_all = stats[1].T[:, None, :]
    delta_all = stats[2].T[:, None, :]

    kq_heads = local_k.reshape(tok_rows, head_count, HD)
    kv_heads = local_v.reshape(tok_rows, head_count, HD)
    key_visible = all_pos[None, :] >= own_pos[:, None]
    scores_t = (
        jnp.einsum("uhd,htd->hut", kq_heads, qa_heads, preferred_element_type=jnp.float32)
        * score_scale
    )
    raw_t = jnp.where(key_visible, jnp.exp(scores_t - top_all), 0.0)
    probs_t = raw_t / total_all
    probs_low_t = probs_t.astype(jnp.bfloat16)
    dprob_t = jnp.einsum("uhd,htd->hut", kv_heads, da_heads, preferred_element_type=jnp.float32)
    dscore_t = (probs_t * (dprob_t - delta_all) * score_scale).astype(jnp.bfloat16)
    grad_k = jnp.einsum("hut,htd->uhd", dscore_t, qa_heads, preferred_element_type=jnp.float32)
    grad_v = jnp.einsum("hut,htd->uhd", probs_low_t, da_heads, preferred_element_type=jnp.float32)
    grad_keys = grad_k.astype(jnp.bfloat16).reshape(tok_rows, channels)
    grad_values = grad_v.astype(jnp.bfloat16).reshape(tok_rows, channels)

    out_pad = padded(attn_out, half_width)
    conv_sum = jnp.zeros((tok_rows, channels), jnp.float32)
    filter_rows = []
    local_gf = local_g.astype(jnp.float32)
    for tap_index in range(TAPS):
        moved = out_pad[tap_index : tap_index + tok_rows].astype(jnp.float32)
        conv_sum = conv_sum + filter_taps[tap_index] * moved
        filter_rows.append(jnp.sum(moved * local_gf, 0))
    filter_gradient = butterfly_sum(jnp.stack(filter_rows, 0))
    conv_output = conv_sum.astype(jnp.bfloat16)
    return (
        conv_output[None],
        grad_queries[None],
        grad_keys[None],
        grad_values[None],
        filter_gradient,
    )


def solution(mesh):
    block = P("dp", "seq", None)
    in_specs = (block, block, block, block, P())
    out_specs = (block, block, block, block, P())
    return jax.shard_map(
        on_device, mesh=mesh, in_specs=in_specs, out_specs=out_specs, check_vma=False
    )
```

```python
import jax
import jax.numpy as jnp
from jax import lax
from jax.sharding import PartitionSpec as P

HD = 128
TAPS = 7


def padded(value, width):
    peers = lax.axis_size("seq")
    length = value.shape[0]
    up = [(i, (i + 1) % peers) for i in range(peers)]
    down = [(j, i) for i, j in up]
    before = lax.ppermute(value[length - width :], "seq", up)
    after = lax.ppermute(value[:width], "seq", down)
    return jnp.concatenate([before, value, after], axis=0)


def butterfly_sum(value):
    axes = ("dp", "seq")
    peers = lax.axis_size("dp") * lax.axis_size("seq")
    bit = 1
    while bit < peers:
        pairs = [(i, i ^ bit) for i in range(peers)]
        value = value + lax.ppermute(value, axes, pairs)
        bit *= 2
    return value


def butterfly_gather(value):
    peers = lax.axis_size("seq")
    index = lax.axis_index("seq")
    bit = 1
    while bit < peers:
        pairs = [(i, i ^ bit) for i in range(peers)]
        other = lax.ppermute(value, "seq", pairs)
        upper = (index & bit) != 0
        value = jnp.where(
            upper,
            jnp.concatenate([other, value], axis=0),
            jnp.concatenate([value, other], axis=0),
        )
        bit *= 2
    return value


def on_device(queries, key_states, value_states, cotangent, filter_taps):
    tok_rows = queries.shape[1]
    channels = queries.shape[2]
    peers = lax.axis_size("seq")
    seq_total = tok_rows * peers
    head_count = channels // HD
    score_scale = HD ** (-0.5)
    half_width = (TAPS - 1) // 2
    local_q = queries[0]
    local_k = key_states[0]
    local_v = value_states[0]
    local_g = cotangent[0]
    grad_pad = padded(local_g, half_width)
    grad_sum = jnp.zeros((tok_rows, channels), jnp.float32)
    for tap_index in range(TAPS):
        start_row = 2 * half_width - tap_index
        grad_sum = grad_sum + filter_taps[tap_index] * grad_pad[
            start_row : start_row + tok_rows
        ].astype(jnp.float32)
    grad_attn = grad_sum.astype(jnp.bfloat16)

    def head_major(matrix):
        return matrix.reshape(tok_rows, head_count, HD).transpose(1, 0, 2)

    k_heads = lax.all_gather(head_major(local_k), "seq", axis=1, tiled=True)
    k_heads, local_v = lax.optimization_barrier((k_heads, local_v))
    v_heads = lax.all_gather(head_major(local_v), "seq", axis=1, tiled=True)

    q_heads = local_q.reshape(tok_rows, head_count, HD)
    d_heads = grad_attn.reshape(tok_rows, head_count, HD)

    device_index = lax.axis_index("seq")
    own_pos = device_index * tok_rows + jnp.arange(tok_rows, dtype=jnp.int32)
    all_pos = jnp.arange(seq_total, dtype=jnp.int32)
    visible = own_pos[:, None] >= all_pos[None, :]

    scores = (
        jnp.einsum("thd,hud->htu", q_heads, k_heads, preferred_element_type=jnp.float32)
        * score_scale
    )
    row_top = jnp.max(jnp.where(visible, scores, -jnp.inf), -1, keepdims=True)
    row_top, local_q2 = lax.optimization_barrier((row_top, local_q))
    qa_heads = lax.all_gather(head_major(local_q2), "seq", axis=1, tiled=True)
    raw = jnp.where(visible, jnp.exp(scores - row_top), 0.0)
    row_total = jnp.sum(raw, -1, keepdims=True)
    probs = raw / row_total
    probs_low = probs.astype(jnp.bfloat16)
    probs_low, grad_attn2 = lax.optimization_barrier((probs_low, grad_attn))
    da_heads = lax.all_gather(head_major(grad_attn2), "seq", axis=1, tiled=True)
    attended = jnp.einsum("htu,hud->thd", probs_low, v_heads, preferred_element_type=jnp.float32)
    attn_out = attended.astype(jnp.bfloat16).reshape(tok_rows, channels)
    dprob = jnp.einsum("thd,hud->htu", d_heads, v_heads, preferred_element_type=jnp.float32)
    row_delta = jnp.sum(probs * dprob, -1, keepdims=True)
    dscore = (probs * (dprob - row_delta) * score_scale).astype(jnp.bfloat16)
    grad_q = jnp.einsum("htu,hud->thd", dscore, k_heads, preferred_element_type=jnp.float32)
    grad_queries = grad_q.astype(jnp.bfloat16).reshape(tok_rows, channels)

    stats = jnp.stack([row_top[..., 0], row_total[..., 0], row_delta[..., 0]], 0)
    stats = butterfly_gather(stats.transpose(2, 0, 1)).transpose(1, 0, 2)
    top_all = stats[0].T[:, None, :]
    total_all = stats[1].T[:, None, :]
    delta_all = stats[2].T[:, None, :]

    kq_heads = head_major(local_k)
    kv_heads = head_major(local_v)
    key_visible = all_pos[None, :] >= own_pos[:, None]
    scores_t = (
        jnp.einsum("hud,htd->hut", kq_heads, qa_heads, preferred_element_type=jnp.float32)
        * score_scale
    )
    raw_t = jnp.where(key_visible, jnp.exp(scores_t - top_all), 0.0)
    probs_t = raw_t / total_all
    probs_low_t = probs_t.astype(jnp.bfloat16)
    dprob_t = jnp.einsum("hud,htd->hut", kv_heads, da_heads, preferred_element_type=jnp.float32)
    dscore_t = (probs_t * (dprob_t - delta_all) * score_scale).astype(jnp.bfloat16)
    grad_k = jnp.einsum("hut,htd->uhd", dscore_t, qa_heads, preferred_element_type=jnp.float32)
    grad_v = jnp.einsum("hut,htd->uhd", probs_low_t, da_heads, preferred_element_type=jnp.float32)
    grad_keys = grad_k.astype(jnp.bfloat16).reshape(tok_rows, channels)
    grad_values = grad_v.astype(jnp.bfloat16).reshape(tok_rows, channels)

    out_pad = padded(attn_out, half_width)
    conv_sum = jnp.zeros((tok_rows, channels), jnp.float32)
    filter_rows = []
    local_gf = local_g.astype(jnp.float32)
    for tap_index in range(TAPS):
        moved = out_pad[tap_index : tap_index + tok_rows].astype(jnp.float32)
        conv_sum = conv_sum + filter_taps[tap_index] * moved
        filter_rows.append(jnp.sum(moved * local_gf, 0))
    filter_gradient = butterfly_sum(jnp.stack(filter_rows, 0))
    conv_output = conv_sum.astype(jnp.bfloat16)
    return (
        conv_output[None],
        grad_queries[None],
        grad_keys[None],
        grad_values[None],
        filter_gradient,
    )


def solution(mesh):
    block = P("dp", "seq", None)
    in_specs = (block, block, block, block, P())
    out_specs = (block, block, block, block, P())
    return jax.shard_map(
        on_device, mesh=mesh, in_specs=in_specs, out_specs=out_specs, check_vma=False
    )
```

```python
import jax
import jax.numpy as jnp
from jax import lax
from jax.sharding import PartitionSpec as P

HD = 128
TAPS = 7


def padded(value, width):
    peers = lax.axis_size("seq")
    length = value.shape[0]
    up = [(i, (i + 1) % peers) for i in range(peers)]
    down = [(j, i) for i, j in up]
    before = lax.ppermute(value[length - width :], "seq", up)
    after = lax.ppermute(value[:width], "seq", down)
    return jnp.concatenate([before, value, after], axis=0)


def butterfly_sum(value):
    axes = ("dp", "seq")
    peers = lax.axis_size("dp") * lax.axis_size("seq")
    bit = 1
    while bit < peers:
        pairs = [(i, i ^ bit) for i in range(peers)]
        value = value + lax.ppermute(value, axes, pairs)
        bit *= 2
    return value


def butterfly_gather(value):
    peers = lax.axis_size("seq")
    index = lax.axis_index("seq")
    bit = 1
    while bit < peers:
        pairs = [(i, i ^ bit) for i in range(peers)]
        other = lax.ppermute(value, "seq", pairs)
        upper = (index & bit) != 0
        value = jnp.where(
            upper,
            jnp.concatenate([other, value], axis=0),
            jnp.concatenate([value, other], axis=0),
        )
        bit *= 2
    return value


def on_device(queries, key_states, value_states, cotangent, filter_taps):
    tok_rows = queries.shape[1]
    channels = queries.shape[2]
    peers = lax.axis_size("seq")
    seq_total = tok_rows * peers
    head_count = channels // HD
    score_scale = HD ** (-0.5)
    half_width = (TAPS - 1) // 2
    local_q = queries[0]
    local_k = key_states[0]
    local_v = value_states[0]
    local_g = cotangent[0]
    grad_pad = padded(local_g, half_width)
    grad_sum = jnp.zeros((tok_rows, channels), jnp.float32)
    for tap_index in range(TAPS):
        start_row = 2 * half_width - tap_index
        grad_sum = grad_sum + filter_taps[tap_index] * grad_pad[
            start_row : start_row + tok_rows
        ].astype(jnp.float32)
    grad_attn = grad_sum.astype(jnp.bfloat16)

    def head_major(matrix):
        return matrix.reshape(tok_rows, head_count, HD).transpose(1, 0, 2)

    k_heads = lax.all_gather(head_major(local_k), "seq", axis=1, tiled=True)
    k_heads, local_v = lax.optimization_barrier((k_heads, local_v))
    v_heads = lax.all_gather(head_major(local_v), "seq", axis=1, tiled=True)

    q_heads = head_major(local_q)
    d_heads = head_major(grad_attn)

    device_index = lax.axis_index("seq")
    own_pos = device_index * tok_rows + jnp.arange(tok_rows, dtype=jnp.int32)
    all_pos = jnp.arange(seq_total, dtype=jnp.int32)
    visible = own_pos[:, None] >= all_pos[None, :]

    scores = (
        jnp.einsum("htd,hud->htu", q_heads, k_heads, preferred_element_type=jnp.float32)
        * score_scale
    )
    row_top = jnp.max(jnp.where(visible, scores, -jnp.inf), -1, keepdims=True)
    row_top, local_q2 = lax.optimization_barrier((row_top, local_q))
    qa_heads = lax.all_gather(head_major(local_q2), "seq", axis=1, tiled=True)
    raw = jnp.where(visible, jnp.exp(scores - row_top), 0.0)
    row_total = jnp.sum(raw, -1, keepdims=True)
    probs = raw / row_total
    probs_low = probs.astype(jnp.bfloat16)
    probs_low, grad_attn2 = lax.optimization_barrier((probs_low, grad_attn))
    da_heads = lax.all_gather(head_major(grad_attn2), "seq", axis=1, tiled=True)
    attended = jnp.einsum("htu,hud->thd", probs_low, v_heads, preferred_element_type=jnp.float32)
    attn_out = attended.astype(jnp.bfloat16).reshape(tok_rows, channels)
    dprob = jnp.einsum("htd,hud->htu", d_heads, v_heads, preferred_element_type=jnp.float32)
    row_delta = jnp.sum(probs * dprob, -1, keepdims=True)
    dscore = (probs * (dprob - row_delta) * score_scale).astype(jnp.bfloat16)
    grad_q = jnp.einsum("htu,hud->thd", dscore, k_heads, preferred_element_type=jnp.float32)
    grad_queries = grad_q.astype(jnp.bfloat16).reshape(tok_rows, channels)

    stats = jnp.stack([row_top[..., 0], row_total[..., 0], row_delta[..., 0]], 0)
    stats = butterfly_gather(stats.transpose(2, 0, 1)).transpose(1, 0, 2)
    top_all = stats[0].T[:, None, :]
    total_all = stats[1].T[:, None, :]
    delta_all = stats[2].T[:, None, :]

    kq_heads = head_major(local_k)
    kv_heads = head_major(local_v)
    key_visible = all_pos[None, :] >= own_pos[:, None]
    scores_t = (
        jnp.einsum("hud,htd->hut", kq_heads, qa_heads, preferred_element_type=jnp.float32)
        * score_scale
    )
    raw_t = jnp.where(key_visible, jnp.exp(scores_t - top_all), 0.0)
    probs_t = raw_t / total_all
    probs_low_t = probs_t.astype(jnp.bfloat16)
    dprob_t = jnp.einsum("hud,htd->hut", kv_heads, da_heads, preferred_element_type=jnp.float32)
    dscore_t = (probs_t * (dprob_t - delta_all) * score_scale).astype(jnp.bfloat16)
    grad_k = jnp.einsum("hut,htd->uhd", dscore_t, qa_heads, preferred_element_type=jnp.float32)
    grad_v = jnp.einsum("hut,htd->uhd", probs_low_t, da_heads, preferred_element_type=jnp.float32)
    grad_keys = grad_k.astype(jnp.bfloat16).reshape(tok_rows, channels)
    grad_values = grad_v.astype(jnp.bfloat16).reshape(tok_rows, channels)

    out_pad = padded(attn_out, half_width)
    conv_sum = jnp.zeros((tok_rows, channels), jnp.float32)
    filter_rows = []
    local_gf = local_g.astype(jnp.float32)
    for tap_index in range(TAPS):
        moved = out_pad[tap_index : tap_index + tok_rows].astype(jnp.float32)
        conv_sum = conv_sum + filter_taps[tap_index] * moved
        filter_rows.append(jnp.sum(moved * local_gf, 0))
    filter_gradient = butterfly_sum(jnp.stack(filter_rows, 0))
    conv_output = conv_sum.astype(jnp.bfloat16)
    return (
        conv_output[None],
        grad_queries[None],
        grad_keys[None],
        grad_values[None],
        filter_gradient,
    )


def solution(mesh):
    block = P("dp", "seq", None)
    in_specs = (block, block, block, block, P())
    out_specs = (block, block, block, block, P())
    return jax.shard_map(
        on_device, mesh=mesh, in_specs=in_specs, out_specs=out_specs, check_vma=False
    )
```
